128 devices in a mesh: row: 8 (over x, core), col: 8 (over z_lo, y), space: 2 (over z_hi).
Axes of the slice: x: 4, y: 4, z: 4 (z_hi: 2, z_lo: 2; z = z_hi * 2 + z_lo), core: 2. Of those that a mesh axis runs over, the one named last changes fastest.
Arguments:
- snapshots: bfloat16 [32768, 8192], P(('row', 'col'), 'space'), may hold values from -10 to 10
- ocean_mask: int32 [8192], P('space'), may hold values 0 or 1
- spread: float32 [], replicated, may hold values from 1 to 2
Outputs:
- affinity: float32 [3, 32768, 512], P(None, ('row', 'col'), 'space')
The draws below stay inside these ranges and needn't reach their ends.
All inputs are finite; a program needn't handle non-finite values. No bound on the sum of `ocean_mask` on one device may be relied on, other than what follows from the above.
Results may differ from the reference program's by a relative error of at most 0.0003.
Values may be sent and summed in bfloat16 or wider, within the bound.
No kernel may reach another device: no remote copies, remote signals or barrier semaphores. Data moves between devices by JAX's collectives and lax.ppermute only.
A program may use at most 64 MiB of HBM per device.

```python
import math
import jax
import jax.numpy as jnp
from jax import lax

BLOCK = 512
LAG = 240
BANDS = 3
NT = 32768
NCELL = 8192
N_COL = 8


def draw_snapshots(key, part):
    times = jnp.arange(NT, dtype=jnp.float32)[:, None]
    total = jnp.zeros((NT, NCELL), jnp.float32)
    two_pi = 2.0 * math.pi
    for index in range(3):
        period = jnp.exp(jax.random.uniform(jax.random.fold_in(key, 10 + index), (1, NCELL), jnp.float32, math.log(12.0), math.log(4096.0)))
        phase = jax.random.uniform(jax.random.fold_in(key, 20 + index), (1, NCELL), jnp.float32, 0.0, two_pi)
        amplitude = jax.random.uniform(jax.random.fold_in(key, 30 + index), (1, NCELL), jnp.float32, 0.25, 0.8)
        total = total + amplitude * jnp.sin(two_pi * jnp.mod(times, period) / period + phase)
    for index in range(4):
        period = jnp.exp(jax.random.uniform(jax.random.fold_in(key, 40 + index), (1, 1), jnp.float32, math.log(168.0), math.log(8192.0)))
        phase = jax.random.uniform(jax.random.fold_in(key, 50 + index), (1, 1), jnp.float32, 0.0, two_pi)
        shape_draw = jnp.clip(jax.random.normal(jax.random.fold_in(key, 60 + index), (1, NCELL), jnp.float32), -2.5, 2.5)
        pattern = 0.5 * shape_draw
        total = total + pattern * jnp.sin(two_pi * jnp.mod(times, period) / period + phase)
    noise = 0.45 * jnp.clip(jax.random.normal(jax.random.fold_in(key, 3), (NT, NCELL), jnp.float32), -4.0, 4.0)
    return (total + noise).astype(jnp.bfloat16)


def touch_ends(entries, stream_key, smallest, high):
    shape = entries.shape
    spot = [jax.random.randint(jax.random.fold_in(stream_key, axis), (), 0, shape[axis]) for axis in range(len(shape))]
    entries = entries.at[tuple(spot)].set(smallest)
    longest = shape.index(max(shape))
    spot[longest] = (spot[longest] + 1) % shape[longest]
    return entries.at[tuple(spot)].set(high)


def setup_inputs(seed: int = 0) -> dict:
    seeds = jax.random.split(jax.random.key(seed), 4)
    snapshots = draw_snapshots(jax.random.fold_in(seeds[3], 71), 0)
    ocean_mask = touch_ends((jax.random.randint(seeds[1], (NCELL,), 0, 4) < 3).astype(jnp.int32), jax.random.fold_in(seeds[1], 1), 0, 1)
    spread = jnp.clip(jnp.exp(jax.random.uniform(seeds[2], (), jnp.float32, math.log(1.0), math.log(2.0))), 1.0, 2.0)
    return dict(snapshots=snapshots, ocean_mask=ocean_mask, spread=spread)


def combine_lags(earlier, later, extent):
    keep = earlier.shape[0] + later.shape[0] - extent - 1
    return earlier[-keep:, -keep:] + later[:keep, :keep]

def lag_sum(distance, window):
    extent = distance.shape[0]
    summed = None
    doubled = distance
    remaining = window
    while remaining:
        if remaining % 2 == 1:
            summed = doubled if summed is None else combine_lags(summed, doubled, extent)
        remaining = remaining // 2
        if remaining:
            doubled = combine_lags(doubled, doubled, extent)
    return summed

def reference(snapshots, ocean_mask, spread):
    masked = snapshots * ocean_mask.astype(jnp.bfloat16)[None, :]
    padded = jnp.concatenate([jnp.zeros((LAG - 1, NCELL), jnp.bfloat16), masked], axis=0).astype(jnp.float32)
    row_norms = lax.optimization_barrier(jnp.sum(padded * padded, axis=1))
    extent = BLOCK + LAG - 1
    nblocks = NT // BLOCK
    denominator = LAG * NCELL * spread

    def one_block(block_id):
        group_id = block_id // N_COL
        slot_id = block_id % N_COL
        row_ext = lax.dynamic_slice_in_dim(padded, (block_id * BLOCK).astype(jnp.int32), extent, 0)
        row_sq = lax.dynamic_slice_in_dim(row_norms, (block_id * BLOCK).astype(jnp.int32), extent, 0)
        band_list = []
        for band_id in range(BANDS):
            partner = group_id * N_COL + (slot_id - band_id + N_COL) % N_COL
            col_ext = lax.dynamic_slice_in_dim(padded, (partner * BLOCK).astype(jnp.int32), extent, 0)
            col_sq = lax.dynamic_slice_in_dim(row_norms, (partner * BLOCK).astype(jnp.int32), extent, 0)
            gram_tile = jnp.dot(row_ext, col_ext.T, precision=lax.Precision.HIGHEST, preferred_element_type=jnp.float32)
            distance = row_sq[:, None] + col_sq[None, :] - 2.0 * gram_tile
            band_list.append(jnp.exp(-lag_sum(distance, LAG) / denominator))
        return jnp.stack(band_list)
    block_ids = jnp.arange(nblocks, dtype=jnp.int32)
    kernel = lax.map(one_block, block_ids)
    degree = lax.optimization_barrier(jnp.sum(kernel, axis=(1, 3)))
    group_ids = block_ids // N_COL
    slot_ids = block_ids % N_COL
    col_list = []
    for band_id in range(BANDS):
        partner = group_ids * N_COL + (slot_ids - band_id + N_COL) % N_COL
        col_list.append(degree[partner])
    column_degrees = jnp.stack(col_list, axis=1)
    factor = float(BANDS * BLOCK)
    affinity = factor * kernel / jnp.sqrt(degree[:, None, :, None] * column_degrees[:, :, None, :])
    return jnp.transpose(affinity, (1, 0, 2, 3)).reshape(BANDS, NT, BLOCK)
```

```python
import jax
import jax.numpy as jnp
from jax import lax
from jax.sharding import PartitionSpec as P

LAG = 240
BANDS = 3


def ring(axis, distance):
    n = lax.axis_size(axis)
    return [(i, (i + distance) % n) for i in range(n)]


def combine_lags(earlier, later, extent):
    keep = earlier.shape[0] + later.shape[0] - extent - 1
    return earlier[-keep:, -keep:] + later[:keep, :keep]


def lag_sum(distance, window):
    extent = distance.shape[0]
    summed = None
    doubled = distance
    remaining = window
    while remaining:
        if remaining % 2 == 1:
            summed = doubled if summed is None else combine_lags(summed, doubled, extent)
        remaining = remaining // 2
        if remaining:
            doubled = combine_lags(doubled, doubled, extent)
    return summed


def square_norms(values):
    return jnp.sum(jnp.square(values.astype(jnp.float32)), axis=1)


def lagged_partial(rows, cols):
    gram_tile = lax.dot_general(
        rows, cols, (((1,), (1,)), ((), ())), preferred_element_type=jnp.float32
    )
    distance = square_norms(rows)[:, None] + square_norms(cols)[None, :] - 2.0 * gram_tile
    return lag_sum(distance, LAG)


def per_device(snapshots, ocean_mask, spread):
    block_rows = snapshots.shape[0]
    cells_dev = snapshots.shape[1]
    hist = LAG - 1
    n_col = lax.axis_size("col")
    n_row = lax.axis_size("row")
    slot = lax.axis_index("col")
    masked = snapshots * ocean_mask.astype(jnp.bfloat16)[None, :]
    tail = masked[block_rows - hist :]
    head = masked[: block_rows - hist]

    flat = ("row", "col")
    to_slot0 = [(n_col * r - 1, n_col * r) for r in range(1, n_row)]
    to_slot7 = [(n_col * r - 1, n_col * r + n_col - 1) for r in range(1, n_row)]
    tail_to_first = lax.ppermute(tail, flat, to_slot0)
    tail_to_last = lax.ppermute(tail, flat, to_slot7)

    up = ring("col", 1)
    down = ring("col", -1)
    tail_prev = lax.ppermute(tail, "col", up)
    own_hist = jnp.where(slot == 0, tail_to_first, tail_prev)
    hist_prev = lax.ppermute(own_hist, "col", up)
    head_prev = lax.ppermute(head, "col", up)
    block_next = lax.ppermute(masked, "col", down)
    hist_next = jnp.where(slot == n_col - 1, tail_to_last, tail)

    own_rows = jnp.concatenate([own_hist, masked], axis=0)
    prev_rows = jnp.concatenate([hist_prev, head_prev, tail_prev], axis=0)
    next_rows = jnp.concatenate([hist_next, block_next], axis=0)

    band0 = lagged_partial(own_rows, own_rows)
    band1 = lagged_partial(own_rows, prev_rows)
    band2_next = lagged_partial(next_rows, prev_rows)
    partial_dist = jnp.stack([band0, band1, band2_next])

    n_space = lax.axis_size("space")
    column_width = block_rows // n_space
    side = lax.axis_index("space")
    start_col = side * column_width
    other_col = (1 - side) * column_width
    mine = lax.dynamic_slice_in_dim(partial_dist, start_col, column_width, 2)
    theirs = lax.dynamic_slice_in_dim(partial_dist, other_col, column_width, 2)
    summed = mine + lax.ppermute(theirs, "space", [(0, 1), (1, 0)])
    band2 = lax.ppermute(summed[2], "col", up)
    lagged = jnp.stack([summed[0], summed[1], band2])

    total_cells = cells_dev * n_space
    kernel = jnp.exp(-lagged / (LAG * total_cells * spread))
    degree = lax.psum(jnp.sum(kernel, axis=(0, 2)), "space")
    degree_half = lax.dynamic_slice_in_dim(degree, start_col, column_width, 0)
    degree_list = [degree_half]
    for offset in range(1, BANDS):
        degree_list.append(lax.ppermute(degree_half, "col", ring("col", offset)))
    column_degrees = jnp.stack(degree_list)
    factor = float(BANDS * block_rows)
    return factor * kernel / jnp.sqrt(degree[None, :, None] * column_degrees[:, None, :])


def solution(mesh):
    placed = (P(("row", "col"), "space"), P("space"), P())
    return jax.shard_map(
        per_device,
        mesh=mesh,
        in_specs=placed,
        out_specs=P(None, ("row", "col"), "space"),
        check_vma=False,
    )
```

```python
import jax
import jax.numpy as jnp
from jax import lax
from jax.sharding import PartitionSpec as P

LAG = 240
BANDS = 3


def ring(axis, distance):
    n = lax.axis_size(axis)
    return [(i, (i + distance) % n) for i in range(n)]


def combine_lags(earlier, later, extent):
    keep = earlier.shape[0] + later.shape[0] - extent - 1
    return earlier[-keep:, -keep:] + later[:keep, :keep]


def lag_sum(distance, window):
    extent = distance.shape[0]
    summed = None
    doubled = distance
    remaining = window
    while remaining:
        if remaining % 2 == 1:
            summed = doubled if summed is None else combine_lags(summed, doubled, extent)
        remaining = remaining // 2
        if remaining:
            doubled = combine_lags(doubled, doubled, extent)
    return summed


def square_norms(values):
    return jnp.sum(jnp.square(values.astype(jnp.float32)), axis=1)


def lagged_partial(rows, cols):
    gram_tile = lax.dot_general(
        rows, cols, (((1,), (1,)), ((), ())), preferred_element_type=jnp.float32
    )
    distance = square_norms(rows)[:, None] + square_norms(cols)[None, :] - 2.0 * gram_tile
    return lag_sum(distance, LAG)


def per_device(snapshots, ocean_mask, spread):
    block_rows = snapshots.shape[0]
    cells_dev = snapshots.shape[1]
    hist = LAG - 1
    n_col = lax.axis_size("col")
    n_row = lax.axis_size("row")
    slot = lax.axis_index("col")
    mask = ocean_mask.astype(jnp.bfloat16)[None, :]
    tail = snapshots[block_rows - hist :]

    flat = ("row", "col")
    to_slot0 = [(n_col * r - 1, n_col * r) for r in range(1, n_row)]
    to_slot7 = [(n_col * r - 1, n_col * r + n_col - 1) for r in range(1, n_row)]
    tail_to_first = lax.ppermute(tail, flat, to_slot0)
    tail_to_last = lax.ppermute(tail, flat, to_slot7)

    up = ring("col", 1)
    down = ring("col", -1)
    block_prev = lax.ppermute(snapshots, "col", up)
    block_next = lax.ppermute(snapshots, "col", down)
    own_hist = jnp.where(slot == 0, tail_to_first, block_prev[block_rows - hist :])
    hist_prev = lax.ppermute(own_hist, "col", up)
    hist_next = jnp.where(slot == n_col - 1, tail_to_last, tail)

    own_rows = jnp.concatenate([own_hist, snapshots], axis=0) * mask
    prev_rows = jnp.concatenate([hist_prev, block_prev], axis=0) * mask
    next_rows = jnp.concatenate([hist_next, block_next], axis=0) * mask

    band0 = lagged_partial(own_rows, own_rows)
    band1 = lagged_partial(own_rows, prev_rows)
    band2_next = lagged_partial(next_rows, prev_rows)

    n_space = lax.axis_size("space")
    column_width = block_rows // n_space
    side = lax.axis_index("space")
    start_col = side * column_width
    other_col = (1 - side) * column_width
    swap = [(0, 1), (1, 0)]
    own_bands = jnp.stack([band0, band1])
    mine = lax.dynamic_slice_in_dim(own_bands, start_col, column_width, 2)
    theirs = lax.dynamic_slice_in_dim(own_bands, other_col, column_width, 2)
    summed = mine + lax.ppermute(theirs, "space", swap)

    cs = ("col", "space")
    same_side = [(n_space * c + p, n_space * ((c + 1) % n_col) + p) for c in range(n_col) for p in range(n_space)]
    cross_side = [(n_space * c + p, n_space * ((c + 1) % n_col) + 1 - p) for c in range(n_col) for p in range(n_space)]
    b2_same = lax.ppermute(lax.dynamic_slice_in_dim(band2_next, start_col, column_width, 1), cs, same_side)
    b2_cross = lax.ppermute(lax.dynamic_slice_in_dim(band2_next, other_col, column_width, 1), cs, cross_side)
    band2 = b2_same + b2_cross
    lagged = jnp.stack([summed[0], summed[1], band2])

    total_cells = cells_dev * n_space
    kernel = jnp.exp(-lagged / (LAG * total_cells * spread))
    part_degree = jnp.sum(kernel, axis=(0, 2))
    degree = part_degree + lax.ppermute(part_degree, "space", swap)
    degree_list = [lax.dynamic_slice_in_dim(degree, start_col, column_width, 0)]
    for offset in range(1, BANDS):
        shift_same = [(n_space * c + p, n_space * ((c + offset) % n_col) + p) for c in range(n_col) for p in range(n_space)]
        shift_cross = [(n_space * c + p, n_space * ((c + offset) % n_col) + 1 - p) for c in range(n_col) for p in range(n_space)]
        d_same = lax.ppermute(lax.dynamic_slice_in_dim(part_degree, start_col, column_width, 0), cs, shift_same)
        d_cross = lax.ppermute(lax.dynamic_slice_in_dim(part_degree, other_col, column_width, 0), cs, shift_cross)
        degree_list.append(d_same + d_cross)
    column_degrees = jnp.stack(degree_list)
    factor = float(BANDS * block_rows)
    return factor * kernel / jnp.sqrt(degree[None, :, None] * column_degrees[:, None, :])


def solution(mesh):
    placed = (P(("row", "col"), "space"), P("space"), P())
    return jax.shard_map(
        per_device,
        mesh=mesh,
        in_specs=placed,
        out_specs=P(None, ("row", "col"), "space"),
        check_vma=False,
    )
```

```python
import jax
import jax.numpy as jnp
from jax import lax
from jax.sharding import PartitionSpec as P

LAG = 240
BANDS = 3


def ring(axis, distance):
    n = lax.axis_size(axis)
    return [(i, (i + distance) % n) for i in range(n)]


def combine_lags(earlier, later, extent):
    keep = earlier.shape[0] + later.shape[0] - extent - 1
    return earlier[-keep:, -keep:] + later[:keep, :keep]


def lag_sum(distance, window):
    extent = distance.shape[0]
    summed = None
    doubled = distance
    remaining = window
    while remaining:
        if remaining % 2 == 1:
            summed = doubled if summed is None else combine_lags(summed, doubled, extent)
        remaining = remaining // 2
        if remaining:
            doubled = combine_lags(doubled, doubled, extent)
    return summed


def square_norms(values):
    return jnp.sum(jnp.square(values.astype(jnp.float32)), axis=1)


def lagged_partial(rows, cols):
    gram_tile = lax.dot_general(
        rows, cols, (((1,), (1,)), ((), ())), preferred_element_type=jnp.float32
    )
    distance = square_norms(rows)[:, None] + square_norms(cols)[None, :] - 2.0 * gram_tile
    return lag_sum(distance, LAG)


def lagged_split(rows, late_cols, early_cols):
    early = lax.dot_general(
        rows, early_cols, (((1,), (1,)), ((), ())), preferred_element_type=jnp.float32
    )
    late = lax.dot_general(
        rows, late_cols, (((1,), (1,)), ((), ())), preferred_element_type=jnp.float32
    )
    gram_tile = jnp.concatenate([late, early], axis=1)
    col_sq = jnp.concatenate([square_norms(late_cols), square_norms(early_cols)])
    distance = square_norms(rows)[:, None] + col_sq[None, :] - 2.0 * gram_tile
    return lag_sum(distance, LAG)


def per_device(snapshots, ocean_mask, spread):
    block_rows = snapshots.shape[0]
    cells_dev = snapshots.shape[1]
    hist = LAG - 1
    n_col = lax.axis_size("col")
    n_row = lax.axis_size("row")
    slot = lax.axis_index("col")
    mask = ocean_mask.astype(jnp.bfloat16)[None, :]
    tail = snapshots[block_rows - hist :]
    head = snapshots[: block_rows - hist]

    flat = ("row", "col")
    to_slot0 = [(n_col * r - 1, n_col * r) for r in range(1, n_row)]
    to_slot7 = [(n_col * r - 1, n_col * r + n_col - 1) for r in range(1, n_row)]
    up = ring("col", 1)
    down = ring("col", -1)
    tail_prev = lax.ppermute(tail, "col", up)
    tail_to_first = lax.ppermute(tail, flat, to_slot0)
    own_hist = jnp.where(slot == 0, tail_to_first, tail_prev)
    hist_prev = lax.ppermute(own_hist, "col", up)
    head_prev = lax.ppermute(head, "col", up)
    block_next = lax.ppermute(snapshots, "col", down)
    tail_to_last = lax.ppermute(tail, flat, to_slot7)
    hist_next = jnp.where(slot == n_col - 1, tail_to_last, tail)

    own_rows = jnp.concatenate([own_hist, snapshots], axis=0) * mask
    prev_early = jnp.concatenate([head_prev, tail_prev], axis=0) * mask
    prev_late = hist_prev * mask
    next_rows = jnp.concatenate([hist_next, block_next], axis=0) * mask

    n_space = lax.axis_size("space")
    column_width = block_rows // n_space
    side = lax.axis_index("space")
    start_col = side * column_width
    other_col = (1 - side) * column_width
    swap = [(0, 1), (1, 0)]

    def space_sum(band):
        mine = lax.dynamic_slice_in_dim(band, start_col, column_width, 1)
        theirs = lax.dynamic_slice_in_dim(band, other_col, column_width, 1)
        return mine + lax.ppermute(theirs, "space", swap)

    band0 = space_sum(lagged_partial(own_rows, own_rows))
    band1 = space_sum(lagged_split(own_rows, prev_late, prev_early))
    band2_next = lagged_split(next_rows, prev_late, prev_early)

    cs = ("col", "space")

    def col_shift(offset, flip):
        return [
            (n_space * c + p, n_space * ((c + offset) % n_col) + (1 - p if flip else p))
            for c in range(n_col)
            for p in range(n_space)
        ]

    b2_same = lax.ppermute(lax.dynamic_slice_in_dim(band2_next, start_col, column_width, 1), cs, col_shift(1, False))
    b2_cross = lax.ppermute(lax.dynamic_slice_in_dim(band2_next, other_col, column_width, 1), cs, col_shift(1, True))
    band2 = b2_same + b2_cross
    lagged = jnp.stack([band0, band1, band2])

    total_cells = cells_dev * n_space
    kernel = jnp.exp(-lagged / (LAG * total_cells * spread))
    part_degree = jnp.sum(kernel, axis=(0, 2))
    degree = part_degree + lax.ppermute(part_degree, "space", swap)
    degree_list = [lax.dynamic_slice_in_dim(degree, start_col, column_width, 0)]
    for offset in range(1, BANDS):
        d_same = lax.ppermute(lax.dynamic_slice_in_dim(part_degree, start_col, column_width, 0), cs, col_shift(offset, False))
        d_cross = lax.ppermute(lax.dynamic_slice_in_dim(part_degree, other_col, column_width, 0), cs, col_shift(offset, True))
        degree_list.append(d_same + d_cross)
    column_degrees = jnp.stack(degree_list)
    factor = float(BANDS * block_rows)
    return factor * kernel / jnp.sqrt(degree[None, :, None] * column_degrees[:, None, :])


def solution(mesh):
    placed = (P(("row", "col"), "space"), P("space"), P())
    return jax.shard_map(
        per_device,
        mesh=mesh,
        in_specs=placed,
        out_specs=P(None, ("row", "col"), "space"),
        check_vma=False,
    )
```

```python
import jax
import jax.numpy as jnp
from jax import lax
from jax.sharding import PartitionSpec as P

LAG = 240
BANDS = 3


def ring(axis, distance):
    n = lax.axis_size(axis)
    return [(i, (i + distance) % n) for i in range(n)]


def combine_lags(earlier, later, extent):
    keep = earlier.shape[0] + later.shape[0] - extent - 1
    return earlier[-keep:, -keep:] + later[:keep, :keep]


def lag_sum(distance, window):
    extent = distance.shape[0]
    summed = None
    doubled = distance
    remaining = window
    while remaining:
        if remaining % 2 == 1:
            summed = doubled if summed is None else combine_lags(summed, doubled, extent)
        remaining = remaining // 2
        if remaining:
            doubled = combine_lags(doubled, doubled, extent)
    return summed


def square_norms(values):
    return jnp.sum(jnp.square(values.astype(jnp.float32)), axis=1)


def lagged_partial(rows, cols):
    gram_tile = lax.dot_general(
        rows, cols, (((1,), (1,)), ((), ())), preferred_element_type=jnp.float32
    )
    distance = square_norms(rows)[:, None] + square_norms(cols)[None, :] - 2.0 * gram_tile
    return lag_sum(distance, LAG)


def gram(rows, cols):
    return lax.dot_general(
        rows, cols, (((1,), (1,)), ((), ())), preferred_element_type=jnp.float32
    )


def lagged_split(rows, late_cols, early_gram, early_sq):
    gram_tile = jnp.concatenate([gram(rows, late_cols), early_gram], axis=1)
    col_sq = jnp.concatenate([square_norms(late_cols), early_sq])
    distance = square_norms(rows)[:, None] + col_sq[None, :] - 2.0 * gram_tile
    return lag_sum(distance, LAG)


def per_device(snapshots, ocean_mask, spread):
    block_rows = snapshots.shape[0]
    cells_dev = snapshots.shape[1]
    hist = LAG - 1
    n_col = lax.axis_size("col")
    n_row = lax.axis_size("row")
    slot = lax.axis_index("col")
    mask = ocean_mask.astype(jnp.bfloat16)[None, :]
    tail = snapshots[block_rows - hist :]
    head = snapshots[: block_rows - hist]

    flat = ("row", "col")
    to_slot0 = [(n_col * r - 1, n_col * r) for r in range(1, n_row)]
    to_slot7 = [(n_col * r - 1, n_col * r + n_col - 1) for r in range(1, n_row)]
    up = ring("col", 1)
    down = ring("col", -1)
    tail_prev = lax.ppermute(tail, "col", up)
    tail_to_first = lax.ppermute(tail, flat, to_slot0)
    head_prev = lax.ppermute(head, "col", up)
    block_next = lax.ppermute(snapshots, "col", down)
    tail_to_last = lax.ppermute(tail, flat, to_slot7)
    own_hist = jnp.where(slot == 0, tail_to_first, tail_prev)
    own_rows = jnp.concatenate([own_hist, snapshots], axis=0) * mask
    band0_part = lagged_partial(own_rows, own_rows)
    hist_send, band0_part = lax.optimization_barrier((own_hist, band0_part))
    hist_prev = lax.ppermute(hist_send, "col", up)
    hist_next = jnp.where(slot == n_col - 1, tail_to_last, tail)
    block_next, _ = lax.optimization_barrier((block_next, band0_part))

    prev_early = jnp.concatenate([head_prev, tail_prev], axis=0) * mask
    next_rows = jnp.concatenate([hist_next, block_next], axis=0) * mask
    early1 = gram(own_rows, prev_early)
    early2 = gram(next_rows, prev_early)
    early_sq = square_norms(prev_early)

    n_space = lax.axis_size("space")
    column_width = block_rows // n_space
    side = lax.axis_index("space")
    start_col = side * column_width
    other_col = (1 - side) * column_width
    swap = [(0, 1), (1, 0)]

    def space_sum(band):
        mine = lax.dynamic_slice_in_dim(band, start_col, column_width, 1)
        theirs = lax.dynamic_slice_in_dim(band, other_col, column_width, 1)
        return mine + lax.ppermute(theirs, "space", swap)

    band0_part, early1, early2, early_sq = lax.optimization_barrier((band0_part, early1, early2, early_sq))
    band0 = space_sum(band0_part)
    prev_late = hist_prev * mask
    band1 = space_sum(lagged_split(own_rows, prev_late, early1, early_sq))
    band2_next = lagged_split(next_rows, prev_late, early2, early_sq)

    cs = ("col", "space")

    def col_shift(offset, flip):
        return [
            (n_space * c + p, n_space * ((c + offset) % n_col) + (1 - p if flip else p))
            for c in range(n_col)
            for p in range(n_space)
        ]

    b2_same = lax.ppermute(lax.dynamic_slice_in_dim(band2_next, start_col, column_width, 1), cs, col_shift(1, False))
    b2_cross = lax.ppermute(lax.dynamic_slice_in_dim(band2_next, other_col, column_width, 1), cs, col_shift(1, True))
    band2 = b2_same + b2_cross
    lagged = jnp.stack([band0, band1, band2])

    total_cells = cells_dev * n_space
    kernel = jnp.exp(-lagged / (LAG * total_cells * spread))
    part_degree = jnp.sum(kernel, axis=(0, 2))
    degree = part_degree + lax.ppermute(part_degree, "space", swap)
    degree_list = [lax.dynamic_slice_in_dim(degree, start_col, column_width, 0)]
    for offset in range(1, BANDS):
        d_same = lax.ppermute(lax.dynamic_slice_in_dim(part_degree, start_col, column_width, 0), cs, col_shift(offset, False))
        d_cross = lax.ppermute(lax.dynamic_slice_in_dim(part_degree, other_col, column_width, 0), cs, col_shift(offset, True))
        degree_list.append(d_same + d_cross)
    column_degrees = jnp.stack(degree_list)
    factor = float(BANDS * block_rows)
    return factor * kernel / jnp.sqrt(degree[None, :, None] * column_degrees[:, None, :])


def solution(mesh):
    placed = (P(("row", "col"), "space"), P("space"), P())
    return jax.shard_map(
        per_device,
        mesh=mesh,
        in_specs=placed,
        out_specs=P(None, ("row", "col"), "space"),
        check_vma=False,
    )
```

```python
import jax
import jax.numpy as jnp
from jax import lax
from jax.sharding import PartitionSpec as P

LAG = 240
BANDS = 3


def ring(axis, distance):
    n = lax.axis_size(axis)
    return [(i, (i + distance) % n) for i in range(n)]


def combine_lags(earlier, later, extent):
    keep = earlier.shape[0] + later.shape[0] - extent - 1
    return earlier[-keep:, -keep:] + later[:keep, :keep]


def lag_sum(distance, window):
    extent = distance.shape[0]
    summed = None
    doubled = distance
    remaining = window
    while remaining:
        if remaining % 2 == 1:
            summed = doubled if summed is None else combine_lags(summed, doubled, extent)
        remaining = remaining // 2
        if remaining:
            doubled = combine_lags(doubled, doubled, extent)
    return summed


def square_norms(values):
    return jnp.sum(jnp.square(values.astype(jnp.float32)), axis=1)


def lagged_partial(rows, cols):
    gram_tile = lax.dot_general(
        rows, cols, (((1,), (1,)), ((), ())), preferred_element_type=jnp.float32
    )
    distance = square_norms(rows)[:, None] + square_norms(cols)[None, :] - 2.0 * gram_tile
    return lag_sum(distance, LAG)


def gram(rows, cols):
    return lax.dot_general(
        rows, cols, (((1,), (1,)), ((), ())), preferred_element_type=jnp.float32
    )


def lagged_split(rows, late_cols, early_gram, early_sq):
    gram_tile = jnp.concatenate([gram(rows, late_cols), early_gram], axis=1)
    col_sq = jnp.concatenate([square_norms(late_cols), early_sq])
    distance = square_norms(rows)[:, None] + col_sq[None, :] - 2.0 * gram_tile
    return lag_sum(distance, LAG)


def per_device(snapshots, ocean_mask, spread):
    block_rows = snapshots.shape[0]
    cells_dev = snapshots.shape[1]
    hist = LAG - 1
    n_col = lax.axis_size("col")
    n_row = lax.axis_size("row")
    slot = lax.axis_index("col")
    mask = ocean_mask.astype(jnp.bfloat16)[None, :]
    tail = snapshots[block_rows - hist :]
    head = snapshots[: block_rows - hist]

    flat = ("row", "col")
    to_slot0 = [(n_col * r - 1, n_col * r) for r in range(1, n_row)]
    to_slot7 = [(n_col * r - 1, n_col * r + n_col - 1) for r in range(1, n_row)]
    up = ring("col", 1)
    down = ring("col", -1)
    tail_prev = lax.ppermute(tail, "col", up)
    tail_to_first = lax.ppermute(tail, flat, to_slot0)
    head_prev = lax.ppermute(head, "col", up)
    block_next = lax.ppermute(snapshots, "col", down)
    tail_to_last = lax.ppermute(tail, flat, to_slot7)
    own_hist = jnp.where(slot == 0, tail_to_first, tail_prev)
    own_rows = jnp.concatenate([own_hist, snapshots], axis=0) * mask
    band0_part = lagged_partial(own_rows, own_rows)
    hist_send, band0_part = lax.optimization_barrier((own_hist, band0_part))
    hist_prev = lax.ppermute(hist_send, "col", up)
    hist_next = jnp.where(slot == n_col - 1, tail_to_last, tail)
    block_next, _ = lax.optimization_barrier((block_next, band0_part))

    prev_early = jnp.concatenate([head_prev, tail_prev], axis=0) * mask
    next_rows = jnp.concatenate([hist_next, block_next], axis=0) * mask
    early1 = gram(own_rows, prev_early)
    early2 = gram(next_rows, prev_early)
    early_sq = square_norms(prev_early)

    n_space = lax.axis_size("space")
    column_width = block_rows // n_space
    side = lax.axis_index("space")
    start_col = side * column_width
    other_col = (1 - side) * column_width
    swap = [(0, 1), (1, 0)]

    def space_sum(band):
        mine = lax.dynamic_slice_in_dim(band, start_col, column_width, 1)
        theirs = lax.dynamic_slice_in_dim(band, other_col, column_width, 1)
        return mine + lax.ppermute(theirs, "space", swap)

    band0 = space_sum(band0_part)
    prev_late = hist_prev * mask
    band1 = space_sum(lagged_split(own_rows, prev_late, early1, early_sq))
    band2_next = lagged_split(next_rows, prev_late, early2, early_sq)

    cs = ("col", "space")

    def col_shift(offset, flip):
        return [
            (n_space * c + p, n_space * ((c + offset) % n_col) + (1 - p if flip else p))
            for c in range(n_col)
            for p in range(n_space)
        ]

    b2_same = lax.ppermute(lax.dynamic_slice_in_dim(band2_next, start_col, column_width, 1), cs, col_shift(1, False))
    b2_cross = lax.ppermute(lax.dynamic_slice_in_dim(band2_next, other_col, column_width, 1), cs, col_shift(1, True))
    band2 = b2_same + b2_cross
    lagged = jnp.stack([band0, band1, band2])

    total_cells = cells_dev * n_space
    kernel = jnp.exp(-lagged / (LAG * total_cells * spread))
    part_degree = jnp.sum(kernel, axis=(0, 2))
    degree = part_degree + lax.ppermute(part_degree, "space", swap)
    degree_list = [lax.dynamic_slice_in_dim(degree, start_col, column_width, 0)]
    for offset in range(1, BANDS):
        d_same = lax.ppermute(lax.dynamic_slice_in_dim(part_degree, start_col, column_width, 0), cs, col_shift(offset, False))
        d_cross = lax.ppermute(lax.dynamic_slice_in_dim(part_degree, other_col, column_width, 0), cs, col_shift(offset, True))
        degree_list.append(d_same + d_cross)
    column_degrees = jnp.stack(degree_list)
    factor = float(BANDS * block_rows)
    return factor * kernel / jnp.sqrt(degree[None, :, None] * column_degrees[:, None, :])


def solution(mesh):
    placed = (P(("row", "col"), "space"), P("space"), P())
    return jax.shard_map(
        per_device,
        mesh=mesh,
        in_specs=placed,
        out_specs=P(None, ("row", "col"), "space"),
        check_vma=False,
    )
```

```python
import jax
import jax.numpy as jnp
from jax import lax
from jax.sharding import PartitionSpec as P

LAG = 240
BANDS = 3


def ring(axis, distance):
    n = lax.axis_size(axis)
    return [(i, (i + distance) % n) for i in range(n)]


def combine_lags(earlier, later, extent):
    keep = earlier.shape[0] + later.shape[0] - extent - 1
    return earlier[-keep:, -keep:] + later[:keep, :keep]


def lag_sum(distance, window):
    extent = distance.shape[0]
    summed = None
    doubled = distance
    remaining = window
    while remaining:
        if remaining % 2 == 1:
            summed = doubled if summed is None else combine_lags(summed, doubled, extent)
        remaining = remaining // 2
        if remaining:
            doubled = combine_lags(doubled, doubled, extent)
    return summed


def square_norms(values):
    return jnp.sum(jnp.square(values.astype(jnp.float32)), axis=1)


def lagged_partial(rows, cols):
    gram_tile = lax.dot_general(
        rows, cols, (((1,), (1,)), ((), ())), preferred_element_type=jnp.float32
    )
    distance = square_norms(rows)[:, None] + square_norms(cols)[None, :] - 2.0 * gram_tile
    return lag_sum(distance, LAG)


def gram(rows, cols):
    return lax.dot_general(
        rows, cols, (((1,), (1,)), ((), ())), preferred_element_type=jnp.float32
    )


def lagged_split(rows, late_cols, early_gram, early_sq):
    gram_tile = jnp.concatenate([gram(rows, late_cols), early_gram], axis=1)
    col_sq = jnp.concatenate([square_norms(late_cols), early_sq])
    distance = square_norms(rows)[:, None] + col_sq[None, :] - 2.0 * gram_tile
    return lag_sum(distance, LAG)


def per_device(snapshots, ocean_mask, spread):
    block_rows = snapshots.shape[0]
    cells_dev = snapshots.shape[1]
    hist = LAG - 1
    n_col = lax.axis_size("col")
    n_row = lax.axis_size("row")
    slot = lax.axis_index("col")
    mask = ocean_mask.astype(jnp.bfloat16)[None, :]
    tail = snapshots[block_rows - hist :]
    head = snapshots[: block_rows - hist]

    flat = ("row", "col")
    to_slot0 = [(n_col * r - 1, n_col * r) for r in range(1, n_row)]
    to_slot7 = [(n_col * r - 1, n_col * r + n_col - 1) for r in range(1, n_row)]
    up = ring("col", 1)
    down = ring("col", -1)
    tail_prev = lax.ppermute(tail, "col", up)
    tail_to_first = lax.ppermute(tail, flat, to_slot0)
    head_prev = lax.ppermute(head, "col", up)
    block_next = lax.ppermute(snapshots, "col", down)
    tail_to_last = lax.ppermute(tail, flat, to_slot7)
    own_hist = jnp.where(slot == 0, tail_to_first, tail_prev)
    own_rows = jnp.concatenate([own_hist, snapshots], axis=0) * mask
    band0_part = lagged_partial(own_rows, own_rows)
    hist_send, band0_part = lax.optimization_barrier((own_hist, band0_part))
    hist_prev = lax.ppermute(hist_send, "col", up)
    hist_next = jnp.where(slot == n_col - 1, tail_to_last, tail)
    block_next, _ = lax.optimization_barrier((block_next, band0_part))

    prev_early = jnp.concatenate([head_prev, tail_prev], axis=0) * mask
    next_rows = jnp.concatenate([hist_next, block_next], axis=0) * mask
    early1 = gram(own_rows, prev_early)
    early2 = gram(next_rows, prev_early)
    early_sq = square_norms(prev_early)

    n_space = lax.axis_size("space")
    column_width = block_rows // n_space
    side = lax.axis_index("space")
    start_col = side * column_width
    other_col = (1 - side) * column_width
    swap = [(0, 1), (1, 0)]

    def space_sum(band):
        mine = lax.dynamic_slice_in_dim(band, start_col, column_width, 1)
        theirs = lax.dynamic_slice_in_dim(band, other_col, column_width, 1)
        return mine + lax.ppermute(theirs, "space", swap)

    band0 = space_sum(band0_part)
    prev_late = hist_prev * mask
    band1_part = lagged_split(own_rows, prev_late, early1, early_sq)
    band1 = space_sum(band1_part)
    prev_late_b2, _ = lax.optimization_barrier((prev_late, band1_part))
    band2_next = lagged_split(next_rows, prev_late_b2, early2, early_sq)

    cs = ("col", "space")

    def col_shift(offset, flip):
        return [
            (n_space * c + p, n_space * ((c + offset) % n_col) + (1 - p if flip else p))
            for c in range(n_col)
            for p in range(n_space)
        ]

    b2_same = lax.ppermute(lax.dynamic_slice_in_dim(band2_next, start_col, column_width, 1), cs, col_shift(1, False))
    b2_cross = lax.ppermute(lax.dynamic_slice_in_dim(band2_next, other_col, column_width, 1), cs, col_shift(1, True))
    band2 = b2_same + b2_cross
    lagged = jnp.stack([band0, band1, band2])

    total_cells = cells_dev * n_space
    kernel = jnp.exp(-lagged / (LAG * total_cells * spread))
    part_degree = jnp.sum(kernel, axis=(0, 2))
    degree = part_degree + lax.ppermute(part_degree, "space", swap)
    degree_list = [lax.dynamic_slice_in_dim(degree, start_col, column_width, 0)]
    for offset in range(1, BANDS):
        d_same = lax.ppermute(lax.dynamic_slice_in_dim(part_degree, start_col, column_width, 0), cs, col_shift(offset, False))
        d_cross = lax.ppermute(lax.dynamic_slice_in_dim(part_degree, other_col, column_width, 0), cs, col_shift(offset, True))
        degree_list.append(d_same + d_cross)
    column_degrees = jnp.stack(degree_list)
    factor = float(BANDS * block_rows)
    return factor * kernel / jnp.sqrt(degree[None, :, None] * column_degrees[:, None, :])


def solution(mesh):
    placed = (P(("row", "col"), "space"), P("space"), P())
    return jax.shard_map(
        per_device,
        mesh=mesh,
        in_specs=placed,
        out_specs=P(None, ("row", "col"), "space"),
        check_vma=False,
    )
```

```python
import jax
import jax.numpy as jnp
from jax import lax
from jax.sharding import PartitionSpec as P

LAG = 240
BANDS = 3


def ring(axis, distance):
    n = lax.axis_size(axis)
    return [(i, (i + distance) % n) for i in range(n)]


def combine_lags(earlier, later, extent):
    keep = earlier.shape[0] + later.shape[0] - extent - 1
    return earlier[-keep:, -keep:] + later[:keep, :keep]


def lag_sum(distance, window):
    extent = distance.shape[0]
    summed = None
    doubled = distance
    remaining = window
    while remaining:
        if remaining % 2 == 1:
            summed = doubled if summed is None else combine_lags(summed, doubled, extent)
        remaining = remaining // 2
        if remaining:
            doubled = combine_lags(doubled, doubled, extent)
    return summed


def square_norms(values):
    return jnp.sum(jnp.square(values.astype(jnp.float32)), axis=1)


def lagged_partial(rows, cols):
    gram_tile = lax.dot_general(
        rows, cols, (((1,), (1,)), ((), ())), preferred_element_type=jnp.float32
    )
    distance = square_norms(rows)[:, None] + square_norms(cols)[None, :] - 2.0 * gram_tile
    return lag_sum(distance, LAG)


def gram(rows, cols):
    return lax.dot_general(
        rows, cols, (((1,), (1,)), ((), ())), preferred_element_type=jnp.float32
    )


def lagged_split(rows, late_cols, early_gram, early_sq):
    gram_tile = jnp.concatenate([gram(rows, late_cols), early_gram], axis=1)
    col_sq = jnp.concatenate([square_norms(late_cols), early_sq])
    distance = square_norms(rows)[:, None] + col_sq[None, :] - 2.0 * gram_tile
    return lag_sum(distance, LAG)


def per_device(snapshots, ocean_mask, spread):
    block_rows = snapshots.shape[0]
    cells_dev = snapshots.shape[1]
    hist = LAG - 1
    n_col = lax.axis_size("col")
    n_row = lax.axis_size("row")
    slot = lax.axis_index("col")
    mask = ocean_mask.astype(jnp.bfloat16)[None, :]
    tail = snapshots[block_rows - hist :]
    head = snapshots[: block_rows - hist]

    flat = ("row", "col")
    to_slot0 = [(n_col * r - 1, n_col * r) for r in range(1, n_row)]
    to_slot7 = [(n_col * r - 1, n_col * r + n_col - 1) for r in range(1, n_row)]
    up = ring("col", 1)
    down = ring("col", -1)
    tail_prev = lax.ppermute(tail, "col", up)
    tail_to_first = lax.ppermute(tail, flat, to_slot0)
    head_prev = lax.ppermute(head, "col", up)
    block_next = lax.ppermute(snapshots, "col", down)
    tail_to_last = lax.ppermute(tail, flat, to_slot7)
    own_hist = jnp.where(slot == 0, tail_to_first, tail_prev)
    own_rows = jnp.concatenate([own_hist, snapshots], axis=0) * mask
    band0_part = lagged_partial(own_rows, own_rows)
    hist_send, band0_part = lax.optimization_barrier((own_hist, band0_part))
    hist_prev = lax.ppermute(hist_send, "col", up)
    hist_next = jnp.where(slot == n_col - 1, tail_to_last, tail)
    block_next, _ = lax.optimization_barrier((block_next, band0_part))

    prev_early = jnp.concatenate([head_prev, tail_prev], axis=0) * mask
    next_rows = jnp.concatenate([hist_next, block_next], axis=0) * mask
    early1 = gram(own_rows, prev_early)
    early2 = gram(next_rows, prev_early)
    early_sq = square_norms(prev_early)

    n_space = lax.axis_size("space")
    column_width = block_rows // n_space
    side = lax.axis_index("space")
    start_col = side * column_width
    other_col = (1 - side) * column_width
    swap = [(0, 1), (1, 0)]

    def space_sum(band):
        mine = lax.dynamic_slice_in_dim(band, start_col, column_width, 1)
        theirs = lax.dynamic_slice_in_dim(band, other_col, column_width, 1)
        return mine + lax.ppermute(theirs, "space", swap)

    band0 = space_sum(band0_part)
    prev_late = hist_prev * mask
    band1 = space_sum(lagged_split(own_rows, prev_late, early1, early_sq))
    band2_next = lagged_split(next_rows, prev_late, early2, early_sq)

    cs = ("col", "space")

    def col_shift(offset, flip):
        return [
            (n_space * c + p, n_space * ((c + offset) % n_col) + (1 - p if flip else p))
            for c in range(n_col)
            for p in range(n_space)
        ]

    b2_same = lax.ppermute(lax.dynamic_slice_in_dim(band2_next, start_col, column_width, 1), cs, col_shift(1, False))
    b2_cross = lax.ppermute(lax.dynamic_slice_in_dim(band2_next, other_col, column_width, 1), cs, col_shift(1, True))
    band2 = b2_same + b2_cross

    total_cells = cells_dev * n_space
    denominator = LAG * total_cells * spread
    kernel_early = jnp.exp(-jnp.stack([band0, band1]) / denominator)
    kernel_late = jnp.exp(-band2 / denominator)
    kernel = jnp.concatenate([kernel_early, kernel_late[None]], axis=0)
    part_degree = jnp.sum(kernel_early, axis=(0, 2)) + jnp.sum(kernel_late, axis=1)
    degree = part_degree + lax.ppermute(part_degree, "space", swap)
    degree_list = [lax.dynamic_slice_in_dim(degree, start_col, column_width, 0)]
    for offset in range(1, BANDS):
        d_same = lax.ppermute(lax.dynamic_slice_in_dim(part_degree, start_col, column_width, 0), cs, col_shift(offset, False))
        d_cross = lax.ppermute(lax.dynamic_slice_in_dim(part_degree, other_col, column_width, 0), cs, col_shift(offset, True))
        degree_list.append(d_same + d_cross)
    column_degrees = jnp.stack(degree_list)
    factor = float(BANDS * block_rows)
    return factor * kernel / jnp.sqrt(degree[None, :, None] * column_degrees[:, None, :])


def solution(mesh):
    placed = (P(("row", "col"), "space"), P("space"), P())
    return jax.shard_map(
        per_device,
        mesh=mesh,
        in_specs=placed,
        out_specs=P(None, ("row", "col"), "space"),
        check_vma=False,
    )
```

```python
import jax
import jax.numpy as jnp
from jax import lax
from jax.sharding import PartitionSpec as P

LAG = 240
BANDS = 3


def ring(axis, distance):
    n = lax.axis_size(axis)
    return [(i, (i + distance) % n) for i in range(n)]


def combine_lags(earlier, later, extent):
    keep = earlier.shape[0] + later.shape[0] - extent - 1
    return earlier[-keep:, -keep:] + later[:keep, :keep]


def lag_sum(distance, window):
    extent = distance.shape[0]
    summed = None
    doubled = distance
    remaining = window
    while remaining:
        if remaining % 2 == 1:
            summed = doubled if summed is None else combine_lags(summed, doubled, extent)
        remaining = remaining // 2
        if remaining:
            doubled = combine_lags(doubled, doubled, extent)
    return summed


def square_norms(values):
    return jnp.sum(jnp.square(values.astype(jnp.float32)), axis=1)


def lagged_partial(rows, cols):
    gram_tile = lax.dot_general(
        rows, cols, (((1,), (1,)), ((), ())), preferred_element_type=jnp.float32
    )
    distance = square_norms(rows)[:, None] + square_norms(cols)[None, :] - 2.0 * gram_tile
    return lag_sum(distance, LAG)


def gram(rows, cols):
    return lax.dot_general(
        rows, cols, (((1,), (1,)), ((), ())), preferred_element_type=jnp.float32
    )


def lag_sum_rect(distance, window):
    rows, cols = distance.shape
    summed = None
    summed_w = 0
    doubled = distance
    width = 1
    remaining = window
    while remaining:
        if remaining % 2 == 1:
            if summed is None:
                summed, summed_w = doubled, width
            else:
                r = rows - summed_w - width + 1
                c = cols - summed_w - width + 1
                summed = summed[width : width + r, width : width + c] + doubled[:r, :c]
                summed_w += width
        remaining = remaining // 2
        if remaining:
            r = rows - 2 * width + 1
            c = cols - 2 * width + 1
            doubled = doubled[width : width + r, width : width + c] + doubled[:r, :c]
            width *= 2
    return summed


def lagged_split(rows, late_cols, early_gram, early_sq):
    row_sq = square_norms(rows)[:, None]
    early_dist = row_sq + early_sq[None, :] - 2.0 * early_gram
    late_dist = row_sq + square_norms(late_cols)[None, :] - 2.0 * gram(rows, late_cols)
    n_late = late_cols.shape[0]
    right = lag_sum_rect(early_dist, LAG)
    left = lag_sum_rect(jnp.concatenate([late_dist, early_dist[:, : LAG - 1]], axis=1), LAG)
    return jnp.concatenate([left[:, :n_late], right], axis=1)


def per_device(snapshots, ocean_mask, spread):
    block_rows = snapshots.shape[0]
    cells_dev = snapshots.shape[1]
    hist = LAG - 1
    n_col = lax.axis_size("col")
    n_row = lax.axis_size("row")
    slot = lax.axis_index("col")
    mask = ocean_mask.astype(jnp.bfloat16)[None, :]
    tail = snapshots[block_rows - hist :]
    head = snapshots[: block_rows - hist]

    flat = ("row", "col")
    to_slot0 = [(n_col * r - 1, n_col * r) for r in range(1, n_row)]
    to_slot7 = [(n_col * r - 1, n_col * r + n_col - 1) for r in range(1, n_row)]
    up = ring("col", 1)
    down = ring("col", -1)
    tail_prev = lax.ppermute(tail, "col", up)
    tail_to_first = lax.ppermute(tail, flat, to_slot0)
    head_prev = lax.ppermute(head, "col", up)
    block_next = lax.ppermute(snapshots, "col", down)
    tail_to_last = lax.ppermute(tail, flat, to_slot7)
    own_hist = jnp.where(slot == 0, tail_to_first, tail_prev)
    own_rows = jnp.concatenate([own_hist, snapshots], axis=0) * mask
    band0_part = lagged_partial(own_rows, own_rows)
    hist_send, band0_part = lax.optimization_barrier((own_hist, band0_part))
    hist_prev = lax.ppermute(hist_send, "col", up)
    hist_next = jnp.where(slot == n_col - 1, tail_to_last, tail)
    block_next, _ = lax.optimization_barrier((block_next, band0_part))

    prev_early = jnp.concatenate([head_prev, tail_prev], axis=0) * mask
    next_rows = jnp.concatenate([hist_next, block_next], axis=0) * mask
    early1 = gram(own_rows, prev_early)
    early2 = gram(next_rows, prev_early)
    early_sq = square_norms(prev_early)

    n_space = lax.axis_size("space")
    column_width = block_rows // n_space
    side = lax.axis_index("space")
    start_col = side * column_width
    other_col = (1 - side) * column_width
    swap = [(0, 1), (1, 0)]

    def space_sum(band):
        mine = lax.dynamic_slice_in_dim(band, start_col, column_width, 1)
        theirs = lax.dynamic_slice_in_dim(band, other_col, column_width, 1)
        return mine + lax.ppermute(theirs, "space", swap)

    band0 = space_sum(band0_part)
    prev_late = hist_prev * mask
    band1 = space_sum(lagged_split(own_rows, prev_late, early1, early_sq))
    band2_next = lagged_split(next_rows, prev_late, early2, early_sq)

    cs = ("col", "space")

    def col_shift(offset, flip):
        return [
            (n_space * c + p, n_space * ((c + offset) % n_col) + (1 - p if flip else p))
            for c in range(n_col)
            for p in range(n_space)
        ]

    b2_same = lax.ppermute(lax.dynamic_slice_in_dim(band2_next, start_col, column_width, 1), cs, col_shift(1, False))
    b2_cross = lax.ppermute(lax.dynamic_slice_in_dim(band2_next, other_col, column_width, 1), cs, col_shift(1, True))
    band2 = b2_same + b2_cross

    total_cells = cells_dev * n_space
    denominator = LAG * total_cells * spread
    kernel_early = jnp.exp(-jnp.stack([band0, band1]) / denominator)
    kernel_late = jnp.exp(-band2 / denominator)
    kernel = jnp.concatenate([kernel_early, kernel_late[None]], axis=0)
    part_degree = jnp.sum(kernel_early, axis=(0, 2)) + jnp.sum(kernel_late, axis=1)
    degree = part_degree + lax.ppermute(part_degree, "space", swap)
    degree_list = [lax.dynamic_slice_in_dim(degree, start_col, column_width, 0)]
    for offset in range(1, BANDS):
        d_same = lax.ppermute(lax.dynamic_slice_in_dim(part_degree, start_col, column_width, 0), cs, col_shift(offset, False))
        d_cross = lax.ppermute(lax.dynamic_slice_in_dim(part_degree, other_col, column_width, 0), cs, col_shift(offset, True))
        degree_list.append(d_same + d_cross)
    column_degrees = jnp.stack(degree_list)
    factor = float(BANDS * block_rows)
    return factor * kernel / jnp.sqrt(degree[None, :, None] * column_degrees[:, None, :])


def solution(mesh):
    placed = (P(("row", "col"), "space"), P("space"), P())
    return jax.shard_map(
        per_device,
        mesh=mesh,
        in_specs=placed,
        out_specs=P(None, ("row", "col"), "space"),
        check_vma=False,
    )
```

```python
import jax
import jax.numpy as jnp
from jax import lax
from jax.sharding import PartitionSpec as P

LAG = 240
BANDS = 3


def ring(axis, distance):
    n = lax.axis_size(axis)
    return [(i, (i + distance) % n) for i in range(n)]


def combine_lags(earlier, later, extent):
    keep = earlier.shape[0] + later.shape[0] - extent - 1
    return earlier[-keep:, -keep:] + later[:keep, :keep]


def lag_sum(distance, window):
    extent = distance.shape[0]
    summed = None
    doubled = distance
    remaining = window
    while remaining:
        if remaining % 2 == 1:
            summed = doubled if summed is None else combine_lags(summed, doubled, extent)
        remaining = remaining // 2
        if remaining:
            doubled = combine_lags(doubled, doubled, extent)
    return summed


def square_norms(values):
    return jnp.sum(jnp.square(values.astype(jnp.float32)), axis=1)


def lagged_partial(rows, cols):
    gram_tile = lax.dot_general(
        rows, cols, (((1,), (1,)), ((), ())), preferred_element_type=jnp.float32
    )
    distance = square_norms(rows)[:, None] + square_norms(cols)[None, :] - 2.0 * gram_tile
    return lag_sum(distance, LAG)


def gram(rows, cols):
    return lax.dot_general(
        rows, cols, (((1,), (1,)), ((), ())), preferred_element_type=jnp.float32
    )


def lag_sum_rect(distance, window):
    rows, cols = distance.shape
    summed = None
    summed_w = 0
    doubled = distance
    width = 1
    remaining = window
    while remaining:
        if remaining % 2 == 1:
            if summed is None:
                summed, summed_w = doubled, width
            else:
                r = rows - summed_w - width + 1
                c = cols - summed_w - width + 1
                summed = summed[width : width + r, width : width + c] + doubled[:r, :c]
                summed_w += width
        remaining = remaining // 2
        if remaining:
            r = rows - 2 * width + 1
            c = cols - 2 * width + 1
            doubled = doubled[width : width + r, width : width + c] + doubled[:r, :c]
            width *= 2
    return summed


def lagged_split(rows, late_cols, early_gram, early_sq):
    row_sq = square_norms(rows)[:, None]
    early_dist = row_sq + early_sq[None, :] - 2.0 * early_gram
    late_dist = row_sq + square_norms(late_cols)[None, :] - 2.0 * gram(rows, late_cols)
    n_late = late_cols.shape[0]
    right = lag_sum_rect(early_dist, LAG)
    left = lag_sum_rect(jnp.concatenate([late_dist, early_dist[:, : LAG - 1]], axis=1), LAG)
    return jnp.concatenate([left[:, :n_late], right], axis=1)


def per_device(snapshots, ocean_mask, spread):
    block_rows = snapshots.shape[0]
    cells_dev = snapshots.shape[1]
    hist = LAG - 1
    n_col = lax.axis_size("col")
    n_row = lax.axis_size("row")
    slot = lax.axis_index("col")
    mask = ocean_mask.astype(jnp.bfloat16)[None, :]
    tail = snapshots[block_rows - hist :]
    head = snapshots[: block_rows - hist]

    flat = ("row", "col")
    to_slot0 = [(n_col * r - 1, n_col * r) for r in range(1, n_row)]
    to_slot7 = [(n_col * r - 1, n_col * r + n_col - 1) for r in range(1, n_row)]
    up = ring("col", 1)
    down = ring("col", -1)
    tail_prev = lax.ppermute(tail, "col", up)
    tail_to_first = lax.ppermute(tail, flat, to_slot0)
    head_prev = lax.ppermute(head, "col", up)
    half_rows = block_rows // 2
    block_next = jnp.concatenate([
        lax.ppermute(snapshots[:half_rows], "col", down),
        lax.ppermute(snapshots[half_rows:], "col", down),
    ], axis=0)
    tail_to_last = lax.ppermute(tail, flat, to_slot7)
    own_hist = jnp.where(slot == 0, tail_to_first, tail_prev)
    own_rows = jnp.concatenate([own_hist, snapshots], axis=0) * mask
    band0_part = lagged_partial(own_rows, own_rows)
    hist_send, band0_part = lax.optimization_barrier((own_hist, band0_part))
    hist_prev = lax.ppermute(hist_send, "col", up)
    hist_next = jnp.where(slot == n_col - 1, tail_to_last, tail)
    block_next, _ = lax.optimization_barrier((block_next, band0_part))

    prev_early = jnp.concatenate([head_prev, tail_prev], axis=0) * mask
    next_rows = jnp.concatenate([hist_next, block_next], axis=0) * mask
    early1 = gram(own_rows, prev_early)
    early2 = gram(next_rows, prev_early)
    early_sq = square_norms(prev_early)

    n_space = lax.axis_size("space")
    column_width = block_rows // n_space
    side = lax.axis_index("space")
    start_col = side * column_width
    other_col = (1 - side) * column_width
    swap = [(0, 1), (1, 0)]

    def space_sum(band):
        mine = lax.dynamic_slice_in_dim(band, start_col, column_width, 1)
        theirs = lax.dynamic_slice_in_dim(band, other_col, column_width, 1)
        return mine + lax.ppermute(theirs, "space", swap)

    band0 = space_sum(band0_part)
    prev_late = hist_prev * mask
    band1 = space_sum(lagged_split(own_rows, prev_late, early1, early_sq))
    band2_next = lagged_split(next_rows, prev_late, early2, early_sq)

    cs = ("col", "space")

    def col_shift(offset, flip):
        return [
            (n_space * c + p, n_space * ((c + offset) % n_col) + (1 - p if flip else p))
            for c in range(n_col)
            for p in range(n_space)
        ]

    b2_same = lax.ppermute(lax.dynamic_slice_in_dim(band2_next, start_col, column_width, 1), cs, col_shift(1, False))
    b2_cross = lax.ppermute(lax.dynamic_slice_in_dim(band2_next, other_col, column_width, 1), cs, col_shift(1, True))
    band2 = b2_same + b2_cross

    total_cells = cells_dev * n_space
    denominator = LAG * total_cells * spread
    kernel_early = jnp.exp(-jnp.stack([band0, band1]) / denominator)
    kernel_late = jnp.exp(-band2 / denominator)
    kernel = jnp.concatenate([kernel_early, kernel_late[None]], axis=0)
    part_degree = jnp.sum(kernel_early, axis=(0, 2)) + jnp.sum(kernel_late, axis=1)
    degree = part_degree + lax.ppermute(part_degree, "space", swap)
    degree_list = [lax.dynamic_slice_in_dim(degree, start_col, column_width, 0)]
    for offset in range(1, BANDS):
        d_same = lax.ppermute(lax.dynamic_slice_in_dim(part_degree, start_col, column_width, 0), cs, col_shift(offset, False))
        d_cross = lax.ppermute(lax.dynamic_slice_in_dim(part_degree, other_col, column_width, 0), cs, col_shift(offset, True))
        degree_list.append(d_same + d_cross)
    column_degrees = jnp.stack(degree_list)
    factor = float(BANDS * block_rows)
    return factor * kernel / jnp.sqrt(degree[None, :, None] * column_degrees[:, None, :])


def solution(mesh):
    placed = (P(("row", "col"), "space"), P("space"), P())
    return jax.shard_map(
        per_device,
        mesh=mesh,
        in_specs=placed,
        out_specs=P(None, ("row", "col"), "space"),
        check_vma=False,
    )
```

```python
import jax
import jax.numpy as jnp
from jax import lax
from jax.sharding import PartitionSpec as P

LAG = 240
BANDS = 3


def ring(axis, distance):
    n = lax.axis_size(axis)
    return [(i, (i + distance) % n) for i in range(n)]


def combine_lags(earlier, later, extent):
    keep = earlier.shape[0] + later.shape[0] - extent - 1
    return earlier[-keep:, -keep:] + later[:keep, :keep]


def lag_sum(distance, window):
    extent = distance.shape[0]
    summed = None
    doubled = distance
    remaining = window
    while remaining:
        if remaining % 2 == 1:
            summed = doubled if summed is None else combine_lags(summed, doubled, extent)
        remaining = remaining // 2
        if remaining:
            doubled = combine_lags(doubled, doubled, extent)
    return summed


def square_norms(values):
    return jnp.sum(jnp.square(values.astype(jnp.float32)), axis=1)


def lagged_partial(rows, cols):
    gram_tile = lax.dot_general(
        rows, cols, (((1,), (1,)), ((), ())), preferred_element_type=jnp.float32
    )
    distance = square_norms(rows)[:, None] + square_norms(cols)[None, :] - 2.0 * gram_tile
    return lag_sum(distance, LAG)


def gram(rows, cols):
    return lax.dot_general(
        rows, cols, (((1,), (1,)), ((), ())), preferred_element_type=jnp.float32
    )


def lag_sum_rect(distance, window):
    rows, cols = distance.shape
    summed = None
    summed_w = 0
    doubled = distance
    width = 1
    remaining = window
    while remaining:
        if remaining % 2 == 1:
            if summed is None:
                summed, summed_w = doubled, width
            else:
                r = rows - summed_w - width + 1
                c = cols - summed_w - width + 1
                summed = summed[width : width + r, width : width + c] + doubled[:r, :c]
                summed_w += width
        remaining = remaining // 2
        if remaining:
            r = rows - 2 * width + 1
            c = cols - 2 * width + 1
            doubled = doubled[width : width + r, width : width + c] + doubled[:r, :c]
            width *= 2
    return summed


def lagged_split(rows, late_cols, early_gram, early_sq):
    row_sq = square_norms(rows)[:, None]
    early_dist = row_sq + early_sq[None, :] - 2.0 * early_gram
    late_dist = row_sq + square_norms(late_cols)[None, :] - 2.0 * gram(rows, late_cols)
    n_late = late_cols.shape[0]
    right = lag_sum_rect(early_dist, LAG)
    left = lag_sum_rect(jnp.concatenate([late_dist, early_dist[:, : LAG - 1]], axis=1), LAG)
    return jnp.concatenate([left[:, :n_late], right], axis=1)


def per_device(snapshots, ocean_mask, spread):
    block_rows = snapshots.shape[0]
    cells_dev = snapshots.shape[1]
    hist = LAG - 1
    n_col = lax.axis_size("col")
    n_row = lax.axis_size("row")
    slot = lax.axis_index("col")
    mask = ocean_mask.astype(jnp.bfloat16)[None, :]
    tail = snapshots[block_rows - hist :]
    head = snapshots[: block_rows - hist]

    flat = ("row", "col")
    to_slot0 = [(n_col * r - 1, n_col * r) for r in range(1, n_row)]
    to_slot7 = [(n_col * r - 1, n_col * r + n_col - 1) for r in range(1, n_row)]
    up = ring("col", 1)
    down = ring("col", -1)
    tail_prev = lax.ppermute(tail, "col", up)
    tail_to_first = lax.ppermute(tail, flat, to_slot0)
    head_prev = lax.ppermute(head, "col", up)
    half_rows = block_rows // 2
    block_next = jnp.concatenate([
        lax.ppermute(snapshots[:half_rows], "col", down),
        lax.ppermute(snapshots[half_rows:], "col", down),
    ], axis=0)
    tail_to_last = lax.ppermute(tail, flat, to_slot7)
    own_hist = jnp.where(slot == 0, tail_to_first, tail_prev)
    own_rows = jnp.concatenate([own_hist, snapshots], axis=0) * mask
    band0_part = lagged_partial(own_rows, own_rows)
    hist_send, band0_part = lax.optimization_barrier((own_hist, band0_part))
    hist_prev = lax.ppermute(hist_send, "col", up)
    hist_next = jnp.where(slot == n_col - 1, tail_to_last, tail)
    block_next, _ = lax.optimization_barrier((block_next, band0_part))

    prev_early = jnp.concatenate([head_prev, tail_prev], axis=0) * mask
    next_rows = jnp.concatenate([hist_next, block_next], axis=0) * mask
    early1 = gram(own_rows, prev_early)
    early2 = gram(next_rows, prev_early)
    early_sq = square_norms(prev_early)

    n_space = lax.axis_size("space")
    column_width = block_rows // n_space
    side = lax.axis_index("space")
    start_col = side * column_width
    other_col = (1 - side) * column_width
    swap = [(0, 1), (1, 0)]

    def space_sum(band):
        mine = lax.dynamic_slice_in_dim(band, start_col, column_width, 1)
        theirs = lax.dynamic_slice_in_dim(band, other_col, column_width, 1)
        return mine + lax.ppermute(theirs, "space", swap)

    band0 = space_sum(band0_part)
    prev_late = hist_prev * mask
    band1_part = lagged_split(own_rows, prev_late, early1, early_sq)
    band1 = space_sum(band1_part)
    prev_late_b2, _ = lax.optimization_barrier((prev_late, band1_part))
    band2_next = lagged_split(next_rows, prev_late_b2, early2, early_sq)

    cs = ("col", "space")

    def col_shift(offset, flip):
        return [
            (n_space * c + p, n_space * ((c + offset) % n_col) + (1 - p if flip else p))
            for c in range(n_col)
            for p in range(n_space)
        ]

    b2_same = lax.ppermute(lax.dynamic_slice_in_dim(band2_next, start_col, column_width, 1), cs, col_shift(1, False))
    b2_cross = lax.ppermute(lax.dynamic_slice_in_dim(band2_next, other_col, column_width, 1), cs, col_shift(1, True))
    band2 = b2_same + b2_cross

    total_cells = cells_dev * n_space
    denominator = LAG * total_cells * spread
    kernel_early = jnp.exp(-jnp.stack([band0, band1]) / denominator)
    kernel_late = jnp.exp(-band2 / denominator)
    kernel = jnp.concatenate([kernel_early, kernel_late[None]], axis=0)
    part_degree = jnp.sum(kernel_early, axis=(0, 2)) + jnp.sum(kernel_late, axis=1)
    degree = part_degree + lax.ppermute(part_degree, "space", swap)
    degree_list = [lax.dynamic_slice_in_dim(degree, start_col, column_width, 0)]
    for offset in range(1, BANDS):
        d_same = lax.ppermute(lax.dynamic_slice_in_dim(part_degree, start_col, column_width, 0), cs, col_shift(offset, False))
        d_cross = lax.ppermute(lax.dynamic_slice_in_dim(part_degree, other_col, column_width, 0), cs, col_shift(offset, True))
        degree_list.append(d_same + d_cross)
    column_degrees = jnp.stack(degree_list)
    factor = float(BANDS * block_rows)
    return factor * kernel / jnp.sqrt(degree[None, :, None] * column_degrees[:, None, :])


def solution(mesh):
    placed = (P(("row", "col"), "space"), P("space"), P())
    return jax.shard_map(
        per_device,
        mesh=mesh,
        in_specs=placed,
        out_specs=P(None, ("row", "col"), "space"),
        check_vma=False,
    )
```

```python
import jax
import jax.numpy as jnp
from jax import lax
from jax.sharding import PartitionSpec as P

LAG = 240
BANDS = 3


def ring(axis, distance):
    n = lax.axis_size(axis)
    return [(i, (i + distance) % n) for i in range(n)]


def combine_lags(earlier, later, extent):
    keep = earlier.shape[0] + later.shape[0] - extent - 1
    return earlier[-keep:, -keep:] + later[:keep, :keep]


def lag_sum(distance, window):
    extent = distance.shape[0]
    summed = None
    doubled = distance
    remaining = window
    while remaining:
        if remaining % 2 == 1:
            summed = doubled if summed is None else combine_lags(summed, doubled, extent)
        remaining = remaining // 2
        if remaining:
            doubled = combine_lags(doubled, doubled, extent)
    return summed


def square_norms(values):
    return jnp.sum(jnp.square(values.astype(jnp.float32)), axis=1)


def lagged_partial(rows, cols):
    gram_tile = lax.dot_general(
        rows, cols, (((1,), (1,)), ((), ())), preferred_element_type=jnp.float32
    )
    distance = square_norms(rows)[:, None] + square_norms(cols)[None, :] - 2.0 * gram_tile
    return lag_sum(distance, LAG)


def gram(rows, cols):
    return lax.dot_general(
        rows, cols, (((1,), (1,)), ((), ())), preferred_element_type=jnp.float32
    )


def lag_sum_rect(distance, window):
    rows, cols = distance.shape
    summed = None
    summed_w = 0
    doubled = distance
    width = 1
    remaining = window
    while remaining:
        if remaining % 2 == 1:
            if summed is None:
                summed, summed_w = doubled, width
            else:
                r = rows - summed_w - width + 1
                c = cols - summed_w - width + 1
                summed = summed[width : width + r, width : width + c] + doubled[:r, :c]
                summed_w += width
        remaining = remaining // 2
        if remaining:
            r = rows - 2 * width + 1
            c = cols - 2 * width + 1
            doubled = doubled[width : width + r, width : width + c] + doubled[:r, :c]
            width *= 2
    return summed


def lagged_split(rows, late_cols, early_gram, early_sq):
    row_sq = square_norms(rows)[:, None]
    early_dist = row_sq + early_sq[None, :] - 2.0 * early_gram
    late_dist = row_sq + square_norms(late_cols)[None, :] - 2.0 * gram(rows, late_cols)
    n_late = late_cols.shape[0]
    right = lag_sum_rect(early_dist, LAG)
    left = lag_sum_rect(jnp.concatenate([late_dist, early_dist[:, : LAG - 1]], axis=1), LAG)
    return jnp.concatenate([left[:, :n_late], right], axis=1)


def per_device(snapshots, ocean_mask, spread):
    block_rows = snapshots.shape[0]
    cells_dev = snapshots.shape[1]
    hist = LAG - 1
    n_col = lax.axis_size("col")
    n_row = lax.axis_size("row")
    slot = lax.axis_index("col")
    mask = ocean_mask.astype(jnp.bfloat16)[None, :]
    tail = snapshots[block_rows - hist :]
    head = snapshots[: block_rows - hist]

    flat = ("row", "col")
    to_slot0 = [(n_col * r - 1, n_col * r) for r in range(1, n_row)]
    to_slot7 = [(n_col * r - 1, n_col * r + n_col - 1) for r in range(1, n_row)]
    up = ring("col", 1)
    down = ring("col", -1)
    tail_prev = lax.ppermute(tail, "col", up)
    tail_to_first = lax.ppermute(tail, flat, to_slot0)
    head_prev = lax.ppermute(head, "col", up)
    half_rows = block_rows // 2
    block_next = jnp.concatenate([
        lax.ppermute(snapshots[:half_rows], "col", down),
        lax.ppermute(snapshots[half_rows:], "col", down),
    ], axis=0)
    tail_to_last = lax.ppermute(tail, flat, to_slot7)
    own_hist = jnp.where(slot == 0, tail_to_first, tail_prev)
    own_rows = jnp.concatenate([own_hist, snapshots], axis=0) * mask
    band0_part = lagged_partial(own_rows, own_rows)
    hist_send, band0_part = lax.optimization_barrier((own_hist, band0_part))
    hist_prev = lax.ppermute(hist_send, "col", up)
    hist_next = jnp.where(slot == n_col - 1, tail_to_last, tail)
    block_next, _ = lax.optimization_barrier((block_next, band0_part))

    prev_early = jnp.concatenate([head_prev, tail_prev], axis=0) * mask
    next_rows = jnp.concatenate([hist_next, block_next], axis=0) * mask
    early1 = gram(own_rows, prev_early)
    early2 = gram(next_rows, prev_early)
    early_sq = square_norms(prev_early)

    n_space = lax.axis_size("space")
    column_width = block_rows // n_space
    side = lax.axis_index("space")
    start_col = side * column_width
    other_col = (1 - side) * column_width
    swap = [(0, 1), (1, 0)]

    def space_sum(band):
        mine = lax.dynamic_slice_in_dim(band, start_col, column_width, 1)
        theirs = lax.dynamic_slice_in_dim(band, other_col, column_width, 1)
        return mine + lax.ppermute(theirs, "space", swap)

    band0 = space_sum(band0_part)
    prev_late = hist_prev * mask
    band1_part = lagged_split(own_rows, prev_late, early1, early_sq)
    band1 = space_sum(band1_part)
    prev_late_b2, _ = lax.optimization_barrier((prev_late, band1_part))
    band2_next = lagged_split(next_rows, prev_late_b2, early2, early_sq)

    cs = ("col", "space")

    def col_shift(offset, flip):
        return [
            (n_space * c + p, n_space * ((c + offset) % n_col) + (1 - p if flip else p))
            for c in range(n_col)
            for p in range(n_space)
        ]

    b2_same = lax.ppermute(lax.dynamic_slice_in_dim(band2_next, start_col, column_width, 1), cs, col_shift(1, False))
    b2_cross = lax.ppermute(lax.dynamic_slice_in_dim(band2_next, other_col, column_width, 1), cs, col_shift(1, True))
    band2 = b2_same + b2_cross

    total_cells = cells_dev * n_space
    denominator = LAG * total_cells * spread
    kernel_early = jnp.exp(-jnp.stack([band0, band1]) / denominator)
    kernel_late = jnp.exp(-band2 / denominator)
    kernel = jnp.concatenate([kernel_early, kernel_late[None]], axis=0)
    part_degree = jnp.sum(kernel_early, axis=(0, 2)) + jnp.sum(kernel_late, axis=1)
    degree = part_degree + lax.ppermute(part_degree, "space", swap)
    degree_half = lax.dynamic_slice_in_dim(degree, start_col, column_width, 0)
    degree_list = [degree_half]
    for offset in range(1, BANDS):
        degree_list.append(lax.ppermute(degree_half, "col", ring("col", offset)))
    column_degrees = jnp.stack(degree_list)
    factor = float(BANDS * block_rows)
    return factor * kernel / jnp.sqrt(degree[None, :, None] * column_degrees[:, None, :])


def solution(mesh):
    placed = (P(("row", "col"), "space"), P("space"), P())
    return jax.shard_map(
        per_device,
        mesh=mesh,
        in_specs=placed,
        out_specs=P(None, ("row", "col"), "space"),
        check_vma=False,
    )
```

```python
import jax
import jax.numpy as jnp
from jax import lax
from jax.sharding import PartitionSpec as P

LAG = 240
BANDS = 3


def ring(axis, distance):
    n = lax.axis_size(axis)
    return [(i, (i + distance) % n) for i in range(n)]


def combine_lags(earlier, later, extent):
    keep = earlier.shape[0] + later.shape[0] - extent - 1
    return earlier[-keep:, -keep:] + later[:keep, :keep]


def lag_sum(distance, window):
    extent = distance.shape[0]
    summed = None
    doubled = distance
    remaining = window
    while remaining:
        if remaining % 2 == 1:
            summed = doubled if summed is None else combine_lags(summed, doubled, extent)
        remaining = remaining // 2
        if remaining:
            doubled = combine_lags(doubled, doubled, extent)
    return summed


def square_norms(values):
    return jnp.sum(jnp.square(values.astype(jnp.float32)), axis=1)


def lagged_partial(rows, cols):
    gram_tile = lax.dot_general(
        rows, cols, (((1,), (1,)), ((), ())), preferred_element_type=jnp.float32
    )
    distance = square_norms(rows)[:, None] + square_norms(cols)[None, :] - 2.0 * gram_tile
    return lag_sum(distance, LAG)


def gram(rows, cols):
    return lax.dot_general(
        rows, cols, (((1,), (1,)), ((), ())), preferred_element_type=jnp.float32
    )


def lag_sum_rect(distance, window):
    rows, cols = distance.shape
    summed = None
    summed_w = 0
    doubled = distance
    width = 1
    remaining = window
    while remaining:
        if remaining % 2 == 1:
            if summed is None:
                summed, summed_w = doubled, width
            else:
                r = rows - summed_w - width + 1
                c = cols - summed_w - width + 1
                summed = summed[width : width + r, width : width + c] + doubled[:r, :c]
                summed_w += width
        remaining = remaining // 2
        if remaining:
            r = rows - 2 * width + 1
            c = cols - 2 * width + 1
            doubled = doubled[width : width + r, width : width + c] + doubled[:r, :c]
            width *= 2
    return summed


def lagged_split(rows, late_cols, early_gram, early_sq):
    row_sq = square_norms(rows)[:, None]
    early_dist = row_sq + early_sq[None, :] - 2.0 * early_gram
    late_dist = row_sq + square_norms(late_cols)[None, :] - 2.0 * gram(rows, late_cols)
    n_late = late_cols.shape[0]
    right = lag_sum_rect(early_dist, LAG)
    left = lag_sum_rect(jnp.concatenate([late_dist, early_dist[:, : LAG - 1]], axis=1), LAG)
    return jnp.concatenate([left[:, :n_late], right], axis=1)


def per_device(snapshots, ocean_mask, spread):
    block_rows = snapshots.shape[0]
    cells_dev = snapshots.shape[1]
    hist = LAG - 1
    n_col = lax.axis_size("col")
    n_row = lax.axis_size("row")
    slot = lax.axis_index("col")
    mask = ocean_mask.astype(jnp.bfloat16)[None, :]
    tail = snapshots[block_rows - hist :]
    head = snapshots[: block_rows - hist]

    flat = ("row", "col")
    to_slot0 = [(n_col * r - 1, n_col * r) for r in range(1, n_row)]
    to_slot7 = [(n_col * r - 1, n_col * r + n_col - 1) for r in range(1, n_row)]
    up = ring("col", 1)
    down = ring("col", -1)
    tail_prev = lax.ppermute(tail, "col", up)
    tail_to_first = lax.ppermute(tail, flat, to_slot0)
    head_prev = lax.ppermute(head, "col", up)
    half_rows = block_rows // 2
    next_first = lax.ppermute(snapshots[:half_rows], "col", down)
    tail_to_last = lax.ppermute(tail, flat, to_slot7)
    own_hist = jnp.where(slot == 0, tail_to_first, tail_prev)
    own_rows = jnp.concatenate([own_hist, snapshots], axis=0) * mask
    band0_part = lagged_partial(own_rows, own_rows)
    hist_prev = lax.ppermute(own_hist, "col", up)
    second_send, band0_part = lax.optimization_barrier((snapshots[half_rows:], band0_part))
    block_next = jnp.concatenate([next_first, lax.ppermute(second_send, "col", down)], axis=0)
    hist_next = jnp.where(slot == n_col - 1, tail_to_last, tail)
    block_next, _ = lax.optimization_barrier((block_next, band0_part))

    prev_early = jnp.concatenate([head_prev, tail_prev], axis=0) * mask
    next_rows = jnp.concatenate([hist_next, block_next], axis=0) * mask
    early1 = gram(own_rows, prev_early)
    early2 = gram(next_rows, prev_early)
    early_sq = square_norms(prev_early)

    n_space = lax.axis_size("space")
    column_width = block_rows // n_space
    side = lax.axis_index("space")
    start_col = side * column_width
    other_col = (1 - side) * column_width
    swap = [(0, 1), (1, 0)]

    def space_sum(band):
        mine = lax.dynamic_slice_in_dim(band, start_col, column_width, 1)
        theirs = lax.dynamic_slice_in_dim(band, other_col, column_width, 1)
        return mine + lax.ppermute(theirs, "space", swap)

    band0 = space_sum(band0_part)
    prev_late = hist_prev * mask
    band1_part = lagged_split(own_rows, prev_late, early1, early_sq)
    band1 = space_sum(band1_part)
    prev_late_b2, _ = lax.optimization_barrier((prev_late, band1_part))
    band2_next = lagged_split(next_rows, prev_late_b2, early2, early_sq)

    cs = ("col", "space")

    def col_shift(offset, flip):
        return [
            (n_space * c + p, n_space * ((c + offset) % n_col) + (1 - p if flip else p))
            for c in range(n_col)
            for p in range(n_space)
        ]

    b2_same = lax.ppermute(lax.dynamic_slice_in_dim(band2_next, start_col, column_width, 1), cs, col_shift(1, False))
    b2_cross = lax.ppermute(lax.dynamic_slice_in_dim(band2_next, other_col, column_width, 1), cs, col_shift(1, True))
    band2 = b2_same + b2_cross

    total_cells = cells_dev * n_space
    denominator = LAG * total_cells * spread
    kernel_early = jnp.exp(-jnp.stack([band0, band1]) / denominator)
    kernel_late = jnp.exp(-band2 / denominator)
    kernel = jnp.concatenate([kernel_early, kernel_late[None]], axis=0)
    part_degree = jnp.sum(kernel_early, axis=(0, 2)) + jnp.sum(kernel_late, axis=1)
    degree = part_degree + lax.ppermute(part_degree, "space", swap)
    degree_half = lax.dynamic_slice_in_dim(degree, start_col, column_width, 0)
    degree_list = [degree_half]
    for offset in range(1, BANDS):
        degree_list.append(lax.ppermute(degree_half, "col", ring("col", offset)))
    column_degrees = jnp.stack(degree_list)
    factor = float(BANDS * block_rows)
    return factor * kernel / jnp.sqrt(degree[None, :, None] * column_degrees[:, None, :])


def solution(mesh):
    placed = (P(("row", "col"), "space"), P("space"), P())
    return jax.shard_map(
        per_device,
        mesh=mesh,
        in_specs=placed,
        out_specs=P(None, ("row", "col"), "space"),
        check_vma=False,
    )
```

```python
import jax
import jax.numpy as jnp
from jax import lax
from jax.sharding import PartitionSpec as P

LAG = 240
BANDS = 3


def ring(axis, distance):
    n = lax.axis_size(axis)
    return [(i, (i + distance) % n) for i in range(n)]


def combine_lags(earlier, later, extent):
    keep = earlier.shape[0] + later.shape[0] - extent - 1
    return earlier[-keep:, -keep:] + later[:keep, :keep]


def lag_sum(distance, window):
    extent = distance.shape[0]
    summed = None
    doubled = distance
    remaining = window
    while remaining:
        if remaining % 2 == 1:
            summed = doubled if summed is None else combine_lags(summed, doubled, extent)
        remaining = remaining // 2
        if remaining:
            doubled = combine_lags(doubled, doubled, extent)
    return summed


def square_norms(values):
    return jnp.sum(jnp.square(values.astype(jnp.float32)), axis=1)


def lagged_partial(rows, cols):
    gram_tile = lax.dot_general(
        rows, cols, (((1,), (1,)), ((), ())), preferred_element_type=jnp.float32
    )
    distance = square_norms(rows)[:, None] + square_norms(cols)[None, :] - 2.0 * gram_tile
    return lag_sum(distance, LAG)


def gram(rows, cols):
    return lax.dot_general(
        rows, cols, (((1,), (1,)), ((), ())), preferred_element_type=jnp.float32
    )


def lag_sum_rect(distance, window):
    rows, cols = distance.shape
    summed = None
    summed_w = 0
    doubled = distance
    width = 1
    remaining = window
    while remaining:
        if remaining % 2 == 1:
            if summed is None:
                summed, summed_w = doubled, width
            else:
                r = rows - summed_w - width + 1
                c = cols - summed_w - width + 1
                summed = summed[width : width + r, width : width + c] + doubled[:r, :c]
                summed_w += width
        remaining = remaining // 2
        if remaining:
            r = rows - 2 * width + 1
            c = cols - 2 * width + 1
            doubled = doubled[width : width + r, width : width + c] + doubled[:r, :c]
            width *= 2
    return summed


def lagged_split(rows, late_cols, early_gram, early_sq):
    row_sq = square_norms(rows)[:, None]
    early_dist = row_sq + early_sq[None, :] - 2.0 * early_gram
    late_dist = row_sq + square_norms(late_cols)[None, :] - 2.0 * gram(rows, late_cols)
    n_late = late_cols.shape[0]
    right = lag_sum_rect(early_dist, LAG)
    left = lag_sum_rect(jnp.concatenate([late_dist, early_dist[:, : LAG - 1]], axis=1), LAG)
    return jnp.concatenate([left[:, :n_late], right], axis=1)


def per_device(snapshots, ocean_mask, spread):
    block_rows = snapshots.shape[0]
    cells_dev = snapshots.shape[1]
    hist = LAG - 1
    n_col = lax.axis_size("col")
    n_row = lax.axis_size("row")
    slot = lax.axis_index("col")
    mask = ocean_mask.astype(jnp.bfloat16)[None, :]
    tail = snapshots[block_rows - hist :]
    head = snapshots[: block_rows - hist]

    flat = ("row", "col")
    to_slot0 = [(n_col * r - 1, n_col * r) for r in range(1, n_row)]
    to_slot7 = [(n_col * r - 1, n_col * r + n_col - 1) for r in range(1, n_row)]
    up = ring("col", 1)
    down = ring("col", -1)
    tail_prev = lax.ppermute(tail, "col", up)
    tail_to_first = lax.ppermute(tail, flat, to_slot0)
    head_prev = lax.ppermute(head, "col", up)
    half_rows = block_rows // 2
    block_next = jnp.concatenate([
        lax.ppermute(snapshots[:half_rows], "col", down),
        lax.ppermute(snapshots[half_rows:], "col", down),
    ], axis=0)
    tail_to_last = lax.ppermute(tail, flat, to_slot7)
    own_hist = jnp.where(slot == 0, tail_to_first, tail_prev)
    own_block = snapshots * mask
    own_hist_m = own_hist * mask
    own_rows = jnp.concatenate([own_hist_m, own_block], axis=0)
    block_gram = gram(own_block, own_block)
    hist_gram = gram(own_hist_m, own_rows)
    gram0 = jnp.concatenate([hist_gram, jnp.concatenate([hist_gram[:, hist:].T, block_gram], axis=1)], axis=0)
    row_sq0 = square_norms(own_rows)
    band0_part = lag_sum(row_sq0[:, None] + row_sq0[None, :] - 2.0 * gram0, LAG)
    hist_send, band0_part = lax.optimization_barrier((own_hist, band0_part))
    hist_prev = lax.ppermute(hist_send, "col", up)
    hist_next = jnp.where(slot == n_col - 1, tail_to_last, tail)
    block_next, _ = lax.optimization_barrier((block_next, band0_part))

    prev_early = jnp.concatenate([head_prev, tail_prev], axis=0) * mask
    next_rows = jnp.concatenate([hist_next, block_next], axis=0) * mask
    early1 = gram(own_rows, prev_early)
    early2 = gram(next_rows, prev_early)
    early_sq = square_norms(prev_early)

    n_space = lax.axis_size("space")
    column_width = block_rows // n_space
    side = lax.axis_index("space")
    start_col = side * column_width
    other_col = (1 - side) * column_width
    swap = [(0, 1), (1, 0)]

    def space_sum(band):
        mine = lax.dynamic_slice_in_dim(band, start_col, column_width, 1)
        theirs = lax.dynamic_slice_in_dim(band, other_col, column_width, 1)
        return mine + lax.ppermute(theirs, "space", swap)

    band0 = space_sum(band0_part)
    prev_late = hist_prev * mask
    band1_part = lagged_split(own_rows, prev_late, early1, early_sq)
    band1 = space_sum(band1_part)
    prev_late_b2, _ = lax.optimization_barrier((prev_late, band1_part))
    band2_next = lagged_split(next_rows, prev_late_b2, early2, early_sq)

    cs = ("col", "space")

    def col_shift(offset, flip):
        return [
            (n_space * c + p, n_space * ((c + offset) % n_col) + (1 - p if flip else p))
            for c in range(n_col)
            for p in range(n_space)
        ]

    b2_same = lax.ppermute(lax.dynamic_slice_in_dim(band2_next, start_col, column_width, 1), cs, col_shift(1, False))
    b2_cross = lax.ppermute(lax.dynamic_slice_in_dim(band2_next, other_col, column_width, 1), cs, col_shift(1, True))
    band2 = b2_same + b2_cross

    total_cells = cells_dev * n_space
    denominator = LAG * total_cells * spread
    kernel_early = jnp.exp(-jnp.stack([band0, band1]) / denominator)
    kernel_late = jnp.exp(-band2 / denominator)
    kernel = jnp.concatenate([kernel_early, kernel_late[None]], axis=0)
    part_degree = jnp.sum(kernel_early, axis=(0, 2)) + jnp.sum(kernel_late, axis=1)
    degree = part_degree + lax.ppermute(part_degree, "space", swap)
    degree_half = lax.dynamic_slice_in_dim(degree, start_col, column_width, 0)
    degree_list = [degree_half]
    for offset in range(1, BANDS):
        degree_list.append(lax.ppermute(degree_half, "col", ring("col", offset)))
    column_degrees = jnp.stack(degree_list)
    factor = float(BANDS * block_rows)
    return factor * kernel / jnp.sqrt(degree[None, :, None] * column_degrees[:, None, :])


def solution(mesh):
    placed = (P(("row", "col"), "space"), P("space"), P())
    return jax.shard_map(
        per_device,
        mesh=mesh,
        in_specs=placed,
        out_specs=P(None, ("row", "col"), "space"),
        check_vma=False,
    )
```

```python
import jax
import jax.numpy as jnp
from jax import lax
from jax.sharding import PartitionSpec as P

LAG = 240
BANDS = 3


def ring(axis, distance):
    n = lax.axis_size(axis)
    return [(i, (i + distance) % n) for i in range(n)]


def combine_lags(earlier, later, extent):
    keep = earlier.shape[0] + later.shape[0] - extent - 1
    return earlier[-keep:, -keep:] + later[:keep, :keep]


def lag_sum(distance, window):
    extent = distance.shape[0]
    summed = None
    doubled = distance
    remaining = window
    while remaining:
        if remaining % 2 == 1:
            summed = doubled if summed is None else combine_lags(summed, doubled, extent)
        remaining = remaining // 2
        if remaining:
            doubled = combine_lags(doubled, doubled, extent)
    return summed


def square_norms(values):
    return jnp.sum(jnp.square(values.astype(jnp.float32)), axis=1)


def lagged_partial(rows, cols):
    gram_tile = lax.dot_general(
        rows, cols, (((1,), (1,)), ((), ())), preferred_element_type=jnp.float32
    )
    distance = square_norms(rows)[:, None] + square_norms(cols)[None, :] - 2.0 * gram_tile
    return lag_sum(distance, LAG)


def gram(rows, cols):
    return lax.dot_general(
        rows, cols, (((1,), (1,)), ((), ())), preferred_element_type=jnp.float32
    )


def lag_sum_rect(distance, window):
    rows, cols = distance.shape
    summed = None
    summed_w = 0
    doubled = distance
    width = 1
    remaining = window
    while remaining:
        if remaining % 2 == 1:
            if summed is None:
                summed, summed_w = doubled, width
            else:
                r = rows - summed_w - width + 1
                c = cols - summed_w - width + 1
                summed = summed[width : width + r, width : width + c] + doubled[:r, :c]
                summed_w += width
        remaining = remaining // 2
        if remaining:
            r = rows - 2 * width + 1
            c = cols - 2 * width + 1
            doubled = doubled[width : width + r, width : width + c] + doubled[:r, :c]
            width *= 2
    return summed


def lagged_split(rows, late_cols, early_gram, early_sq):
    row_sq = square_norms(rows)[:, None]
    early_dist = row_sq + early_sq[None, :] - 2.0 * early_gram
    late_dist = row_sq + square_norms(late_cols)[None, :] - 2.0 * gram(rows, late_cols)
    n_late = late_cols.shape[0]
    right = lag_sum_rect(early_dist, LAG)
    left = lag_sum_rect(jnp.concatenate([late_dist, early_dist[:, : LAG - 1]], axis=1), LAG)
    return jnp.concatenate([left[:, :n_late], right], axis=1)


def per_device(snapshots, ocean_mask, spread):
    block_rows = snapshots.shape[0]
    cells_dev = snapshots.shape[1]
    hist = LAG - 1
    n_col = lax.axis_size("col")
    n_row = lax.axis_size("row")
    slot = lax.axis_index("col")
    mask = ocean_mask.astype(jnp.bfloat16)[None, :]
    tail = snapshots[block_rows - hist :]
    head = snapshots[: block_rows - hist]

    flat = ("row", "col")
    to_slot0 = [(n_col * r - 1, n_col * r) for r in range(1, n_row)]
    to_slot7 = [(n_col * r - 1, n_col * r + n_col - 1) for r in range(1, n_row)]
    up = ring("col", 1)
    down = ring("col", -1)
    tail_prev = lax.ppermute(tail, "col", up)
    tail_to_first = lax.ppermute(tail, flat, to_slot0)
    head_prev = lax.ppermute(head, "col", up)
    half_rows = block_rows // 2
    block_next = jnp.concatenate([
        lax.ppermute(snapshots[:half_rows], "col", down),
        lax.ppermute(snapshots[half_rows:], "col", down),
    ], axis=0)
    tail_to_last = lax.ppermute(tail, flat, to_slot7)
    own_hist = jnp.where(slot == 0, tail_to_first, tail_prev)
    own_rows = jnp.concatenate([own_hist, snapshots], axis=0) * mask
    band0_part = lagged_partial(own_rows, own_rows)
    hist_send, band0_part = lax.optimization_barrier((own_hist, band0_part))
    hist_prev = lax.ppermute(hist_send, "col", up)
    hist_next = jnp.where(slot == n_col - 1, tail_to_last, tail)
    block_next, _ = lax.optimization_barrier((block_next, band0_part))

    prev_early = jnp.concatenate([head_prev, tail_prev], axis=0) * mask
    next_rows = jnp.concatenate([hist_next, block_next], axis=0) * mask
    early1 = gram(own_rows, prev_early)
    early2 = gram(next_rows, prev_early)
    early_sq = square_norms(prev_early)

    n_space = lax.axis_size("space")
    column_width = block_rows // n_space
    side = lax.axis_index("space")
    start_col = side * column_width
    other_col = (1 - side) * column_width
    swap = [(0, 1), (1, 0)]

    def space_sum(band):
        mine = lax.dynamic_slice_in_dim(band, start_col, column_width, 1)
        theirs = lax.dynamic_slice_in_dim(band, other_col, column_width, 1)
        return mine + lax.ppermute(theirs, "space", swap)

    band0 = space_sum(band0_part)
    prev_late = hist_prev * mask
    band1_part = lagged_split(own_rows, prev_late, early1, early_sq)
    band2_next = lagged_split(next_rows, prev_late, early2, early_sq)
    late_bands = jnp.stack([band1_part, band2_next])
    mine = lax.dynamic_slice_in_dim(late_bands, start_col, column_width, 2)
    theirs = lax.dynamic_slice_in_dim(late_bands, other_col, column_width, 2)
    late_summed = mine + lax.ppermute(theirs, "space", swap)
    band1 = late_summed[0]
    band2 = lax.ppermute(late_summed[1], "col", up)

    total_cells = cells_dev * n_space
    denominator = LAG * total_cells * spread
    kernel_early = jnp.exp(-jnp.stack([band0, band1]) / denominator)
    kernel_late = jnp.exp(-band2 / denominator)
    kernel = jnp.concatenate([kernel_early, kernel_late[None]], axis=0)
    part_degree = jnp.sum(kernel_early, axis=(0, 2)) + jnp.sum(kernel_late, axis=1)
    degree = part_degree + lax.ppermute(part_degree, "space", swap)
    degree_half = lax.dynamic_slice_in_dim(degree, start_col, column_width, 0)
    degree_list = [degree_half]
    for offset in range(1, BANDS):
        degree_list.append(lax.ppermute(degree_half, "col", ring("col", offset)))
    column_degrees = jnp.stack(degree_list)
    factor = float(BANDS * block_rows)
    return factor * kernel / jnp.sqrt(degree[None, :, None] * column_degrees[:, None, :])


def solution(mesh):
    placed = (P(("row", "col"), "space"), P("space"), P())
    return jax.shard_map(
        per_device,
        mesh=mesh,
        in_specs=placed,
        out_specs=P(None, ("row", "col"), "space"),
        check_vma=False,
    )
```
